128 devices in a mesh: row: 8 (over x, core), col: 16 (over z, y).
Axes of the slice: x: 4, y: 4, z: 4, core: 2. Of those that a mesh axis runs over, the one named last changes fastest.
Arguments:
- basis: bfloat16 [32768, 256], P(('row', 'col')), may hold values from -6 to 6
- degree_scale: float32 [32768], P(('row', 'col')), may hold values from 0.5 to 3
- tile_data: bfloat16 [256, 16, 8, 128, 128], P('row', 'col'), may hold values from -0.09375 to 0.09375
- tile_index: int32 [256, 16, 8], P('row', 'col'), may hold values from 0 to 15, as said below
- tile_count: int32 [256, 16], P('row', 'col'), may hold values from 1 to 8, as said below
Outputs:
- embedding: float32 [32768, 256], P(('row', 'col'))
- factor: float32 [256, 256], replicated
The draws below stay inside these ranges and needn't reach their ends.
Inputs may be any that keep to these rules, and one draw needn't show every extreme that they name: `tile_index`: all 8 entries of one tile row in one column block are distinct. `tile_count`: some tile row has 8 live slots in every draw; loads differ widely between devices.
All inputs are finite; a program needn't handle non-finite values.
Results may differ from the reference program's by a relative error of at most 0.034.
Values may be sent and summed in bfloat16 or wider, within the bound.
No kernel may reach another device: no remote copies, remote signals or barrier semaphores. Data moves between devices by JAX's collectives and lax.ppermute only.
A program may use at most 128 MiB of HBM per device.

```python
import math
import jax
import jax.numpy as jnp
from jax import lax

K = 256
TILE = 128
SLOTS = 8
ROW_TILES_DEV = 2
ITERS = 4
ROWS_DEV = 256
NODES = 32768
TROWS = 256
TCOLS = 16
N_ROW = 8
N_COL = 16


def draw_degree_scale(key, part):
    position = jnp.arange(NODES, dtype=jnp.float32) / NODES
    spread = jax.random.uniform(key, (NODES,), jnp.float32, math.log(0.7), math.log(1.4))
    rise = position * math.log(1.8)
    return jnp.exp(spread + rise)


def draw_tile_index(key, part):
    scores = jax.random.randint(key, (TROWS, N_COL, TCOLS), 0, 1 << 20) * TCOLS + jnp.arange(TCOLS)
    order = jnp.argsort(scores, axis=-1)
    return order[..., :SLOTS].astype(jnp.int32)


def draw_tile_count(key, part):
    keys = jax.random.split(key, 5)
    row_tiles = N_COL * ROW_TILES_DEV
    first = jax.random.randint(keys[0], (N_ROW, 1, N_COL), 1, SLOTS + 1)
    second = jax.random.randint(keys[1], (N_ROW, 1, N_COL), 1, SLOTS + 1)
    level = jnp.maximum(first * second // SLOTS, 1)
    busy = jax.random.randint(keys[2], (), 0, N_ROW * N_COL)
    device_ids = jnp.arange(N_ROW * N_COL).reshape(N_ROW, 1, N_COL)
    level = jnp.where(device_ids == busy, SLOTS, level)
    counts = jax.random.randint(keys[3], (N_ROW, row_tiles, N_COL), (level + 1) // 2, level + 1)
    fullest = jax.random.randint(keys[4], (N_ROW, 1, N_COL), 0, row_tiles)
    counts = jnp.where(jnp.arange(row_tiles)[None, :, None] == fullest, level, counts)
    return counts.reshape(TROWS, N_COL).astype(jnp.int32)


def level_of(key, dims, pieces, low, high):
    def one(dim, blocks):
        draws = jax.random.uniform(jax.random.fold_in(jax.random.fold_in(key, 6), dim), (blocks,), jnp.float32, low / len(pieces), high / len(pieces))
        return jnp.repeat(jnp.exp(draws), dims[dim] // blocks).reshape((-1,) + (1,) * (len(dims) - dim - 1))

    factor_of = one(*pieces[0])
    for cut in pieces[1:]:
        factor_of = factor_of * one(*cut)
    return factor_of


def noise(key, extent, width, bound, cuts=(), kind=jnp.bfloat16):
    level = level_of(key, extent, cuts, -0.22, 0.18) if cuts else 1.0
    result = jax.random.normal(key, extent, jnp.float32) * width * level
    return jnp.minimum(jnp.maximum(result, -bound), bound).astype(kind)


def setup_inputs(seed: int = 0) -> dict:
    arg_keys = jax.random.split(jax.random.key(seed), 6)
    basis = noise(arg_keys[0], (NODES, K), 1.0, 6.0, ((0, 128),))
    degree_scale = draw_degree_scale(jax.random.fold_in(arg_keys[5], 71), 0)
    tile_data = noise(arg_keys[2], (TROWS, N_COL, SLOTS, TILE, TILE), (N_COL * SLOTS * TILE // 4) ** -0.5, 0.09375, ((0, 8), (1, 16)))
    tile_index = draw_tile_index(jax.random.fold_in(arg_keys[5], 71), 0)
    tile_count = draw_tile_count(jax.random.fold_in(arg_keys[5], 71), 0)
    return dict(basis=basis, degree_scale=degree_scale, tile_data=tile_data, tile_index=tile_index, tile_count=tile_count)


def apply_operator(probe, tile_data, tile_index, tile_count):
    blocks = probe.reshape(N_ROW, N_COL, ROWS_DEV, K).transpose(1, 0, 2, 3).reshape(N_COL, TCOLS, TILE, K)
    slot_ids = jnp.arange(SLOTS)
    col_ids = jnp.arange(N_COL)

    def one_row(packed):
        tiles, chosen_index, live_count = packed
        chosen = blocks[col_ids[:, None], chosen_index]
        alive = slot_ids[None, :] < live_count[:, None]
        chosen = jnp.where(alive[:, :, None, None], chosen.astype(jnp.float32), jnp.float32(0.0))
        term = jnp.einsum('jsab,jsbk->jak', tiles.astype(jnp.float32), chosen)
        term = lax.optimization_barrier(term.astype(jnp.bfloat16)).astype(jnp.float32)
        return jnp.sum(term, axis=0)
    rows = lax.map(one_row, (tile_data, tile_index, tile_count))
    return rows.reshape(NODES, K)

def reference(basis, degree_scale, tile_data, tile_index, tile_count):
    scale = degree_scale[:, None]
    probe = (basis.astype(jnp.float32) * scale).astype(jnp.bfloat16)
    embedding = None
    factor = None
    for step in range(ITERS):
        image = apply_operator(probe, tile_data, tile_index, tile_count) * scale
        gram = lax.dot_general(image, image, (((0,), (0,)), ((), ())), precision=lax.Precision.HIGHEST) / NODES
        lower = jnp.linalg.cholesky(gram)
        embedding = jax.scipy.linalg.solve_triangular(lower, image.T, lower=True).T
        factor = lower.T
        probe = (embedding * scale).astype(jnp.bfloat16)
    return (embedding, factor)
```

```python
import jax
import jax.numpy as jnp
from jax import lax
from jax.sharding import PartitionSpec as P

ITERS = 4


def gram_of(image, nodes):
    return (
        lax.dot_general(
            image,
            image,
            (((0,), (0,)), ((), ())),
            precision=lax.Precision.HIGHEST,
            preferred_element_type=jnp.float32,
        )
        / nodes
    )


def normalize(image, gram):
    lower = jnp.linalg.cholesky(gram)
    solved = jax.scipy.linalg.solve_triangular(lower, image.T, lower=True).T
    return (solved, lower.T)


def gather_rows(x, axis):
    n = lax.axis_size(axis)
    got = lax.all_to_all(jnp.broadcast_to(x, (n,) + x.shape), axis, 0, 0, tiled=False)
    return got.reshape((-1,) + x.shape[1:])


def sum_scatter_rows(x, axis):
    n = lax.axis_size(axis)
    got = lax.all_to_all(x.reshape((n, -1) + x.shape[1:]), axis, 0, 0, tiled=False)
    return jnp.sum(got.astype(jnp.float32), axis=0)


def sum_all(x, axes):
    n = 1
    for a in axes:
        n *= lax.axis_size(a)
    piece = jnp.sum(lax.all_to_all(x.reshape(n, -1), axes, 0, 0, tiled=False), axis=0)
    full = lax.all_to_all(jnp.broadcast_to(piece, (n,) + piece.shape), axes, 0, 0, tiled=False)
    return full.reshape(x.shape)


def body(basis, degree_scale, tile_data, tile_index, tile_count):
    tiles = tile_data[:, 0]
    index = tile_index[:, 0]
    counts = tile_count[:, 0]
    rows_dev, width = basis.shape
    tile = tiles.shape[-1]
    slots = tiles.shape[1]
    nodes = rows_dev * lax.axis_size("row") * lax.axis_size("col")
    live = jnp.arange(slots)[None, :] < counts[:, None]
    scale = degree_scale[:, None]
    probe = (basis.astype(jnp.float32) * scale).astype(jnp.bfloat16)
    current = probe
    embedding = None
    factor = None
    for step in range(ITERS):
        block_basis = gather_rows(current, "row")
        tiled = block_basis.reshape(-1, tile, width)
        number = lax.axis_size("col") * rows_dev // tile
        chosen = jnp.where(live[:, :, None, None], tiled[index], jnp.zeros((), jnp.bfloat16))
        result = lax.dot_general(
            tiles, chosen, (((1, 3), (1, 2)), ((0,), (0,))), preferred_element_type=jnp.float32
        )
        summed = sum_scatter_rows(result.reshape(number * tile, width).astype(jnp.bfloat16), "col")
        image = summed * scale
        gram = sum_all(gram_of(image, nodes), ("row", "col"))
        embedding, factor = normalize(image, gram)
        current = (embedding * scale).astype(jnp.bfloat16)
    return (embedding, factor)


def solution(mesh):
    placed = (
        P(("row", "col"), None),
        P(("row", "col")),
        P("row", "col", None, None, None),
        P("row", "col", None),
        P("row", "col"),
    )
    return jax.shard_map(
        body, mesh=mesh, in_specs=placed, out_specs=(P(("row", "col"), None), P()), check_vma=False
    )
```

```python
import jax
import jax.numpy as jnp
from jax import lax
from jax.sharding import PartitionSpec as P

ITERS = 4


def gram_of(image, nodes):
    return (
        lax.dot_general(
            image,
            image,
            (((0,), (0,)), ((), ())),
            precision=lax.Precision.HIGHEST,
            preferred_element_type=jnp.float32,
        )
        / nodes
    )


def dot_hi(a, b):
    return jnp.dot(a, b, precision=lax.Precision.HIGHEST, preferred_element_type=jnp.float32)


def cholesky_and_inverse(g, leaf=128):
    n = g.shape[0]
    if n <= leaf:
        lower = jnp.linalg.cholesky(g)
        eye = jnp.eye(n, dtype=jnp.float32)
        return lower, jax.scipy.linalg.solve_triangular(lower, eye, lower=True)
    h = n // 2
    l11, i11 = cholesky_and_inverse(g[:h, :h], leaf)
    l21 = dot_hi(g[h:, :h], i11.T)
    l22, i22 = cholesky_and_inverse(g[h:, h:] - dot_hi(l21, l21.T), leaf)
    i21 = -dot_hi(i22, dot_hi(l21, i11))
    zero = jnp.zeros((h, n - h), jnp.float32)
    lower = jnp.block([[l11, zero], [l21, l22]])
    inverse = jnp.block([[i11, zero], [i21, i22]])
    return lower, inverse


def normalize(image, gram):
    gram = (gram + gram.T) * 0.5
    lower, inverse = cholesky_and_inverse(gram)
    return (dot_hi(image, inverse.T), lower.T)


def gather_rows(x, axis):
    n = lax.axis_size(axis)
    got = lax.all_to_all(jnp.broadcast_to(x, (n,) + x.shape), axis, 0, 0, tiled=False)
    return got.reshape((-1,) + x.shape[1:])


def sum_scatter_rows(x, axis):
    n = lax.axis_size(axis)
    got = lax.all_to_all(x.reshape((n, -1) + x.shape[1:]), axis, 0, 0, tiled=False)
    return jnp.sum(got.astype(jnp.float32), axis=0)


def sum_all(x, axes):
    n = 1
    for a in axes:
        n *= lax.axis_size(a)
    piece = jnp.sum(lax.all_to_all(x.reshape(n, -1), axes, 0, 0, tiled=False), axis=0)
    full = lax.all_to_all(jnp.broadcast_to(piece, (n,) + piece.shape), axes, 0, 0, tiled=False)
    return full.reshape(x.shape)


def body(basis, degree_scale, tile_data, tile_index, tile_count):
    tiles = tile_data[:, 0]
    index = tile_index[:, 0]
    counts = tile_count[:, 0]
    rows_dev, width = basis.shape
    tile = tiles.shape[-1]
    slots = tiles.shape[1]
    nodes = rows_dev * lax.axis_size("row") * lax.axis_size("col")
    live = jnp.arange(slots)[None, :] < counts[:, None]
    scale = degree_scale[:, None]
    probe = (basis.astype(jnp.float32) * scale).astype(jnp.bfloat16)
    number = lax.axis_size("col") * rows_dev // tile

    def one_step(current):
        block_basis = gather_rows(current, "row")
        tiled = block_basis.reshape(-1, tile, width)
        chosen = jnp.where(live[:, :, None, None], tiled[index], jnp.zeros((), jnp.bfloat16))
        result = lax.dot_general(
            tiles, chosen, (((1, 3), (1, 2)), ((0,), (0,))), preferred_element_type=jnp.float32
        )
        summed = sum_scatter_rows(result.reshape(number * tile, width).astype(jnp.bfloat16), "col")
        image = summed * scale
        gram = sum_all(gram_of(image, nodes), ("row", "col"))
        return normalize(image, gram)

    def loop_step(i, carry):
        embedding, factor = one_step(carry[0])
        return ((embedding * scale).astype(jnp.bfloat16), embedding, factor)

    start = (probe, jnp.zeros(basis.shape, jnp.float32), jnp.zeros((width, width), jnp.float32))
    _, embedding, factor = lax.fori_loop(0, ITERS, loop_step, start)
    return (embedding, factor)

    embedding, factor = one_step(probe)
    embedding, factor = lax.fori_loop(1, ITERS, loop_step, (embedding, factor))
    return (embedding, factor)


def solution(mesh):
    placed = (
        P(("row", "col"), None),
        P(("row", "col")),
        P("row", "col", None, None, None),
        P("row", "col", None),
        P("row", "col"),
    )
    return jax.shard_map(
        body, mesh=mesh, in_specs=placed, out_specs=(P(("row", "col"), None), P()), check_vma=False
    )
```

```python
import functools

import jax
import jax.numpy as jnp
from jax import lax
from jax.experimental import pallas as pl
from jax.experimental.pallas import tpu as pltpu
from jax.sharding import PartitionSpec as P

ITERS = 4


def gram_of(image, nodes):
    return (
        lax.dot_general(
            image,
            image,
            (((0,), (0,)), ((), ())),
            precision=lax.Precision.HIGHEST,
            preferred_element_type=jnp.float32,
        )
        / nodes
    )


def dot_hi(a, b):
    return jnp.dot(a, b, precision=lax.Precision.HIGHEST, preferred_element_type=jnp.float32)


def cholesky_and_inverse(g, leaf=128):
    n = g.shape[0]
    if n <= leaf:
        lower = jnp.linalg.cholesky(g)
        eye = jnp.eye(n, dtype=jnp.float32)
        return lower, jax.scipy.linalg.solve_triangular(lower, eye, lower=True)
    h = n // 2
    l11, i11 = cholesky_and_inverse(g[:h, :h], leaf)
    l21 = dot_hi(g[h:, :h], i11.T)
    l22, i22 = cholesky_and_inverse(g[h:, h:] - dot_hi(l21, l21.T), leaf)
    i21 = -dot_hi(i22, dot_hi(l21, i11))
    zero = jnp.zeros((h, n - h), jnp.float32)
    lower = jnp.block([[l11, zero], [l21, l22]])
    inverse = jnp.block([[i11, zero], [i21, i22]])
    return lower, inverse


def normalize(image, gram):
    gram = (gram + gram.T) * 0.5
    lower, inverse = cholesky_and_inverse(gram)
    return (dot_hi(image, inverse.T), lower.T)


def _apply_kernel(index_ref, count_ref, tiles_ref, basis_ref, out_ref, gat_ref, *, rows_per_block, slots, tile):
    block = pl.program_id(0)
    for r in range(rows_per_block):
        t = block * rows_per_block + r
        live = count_ref[t]
        for s in range(slots):
            start = pl.multiple_of(index_ref[t * slots + s] * tile, tile)
            rows = basis_ref[pl.ds(start, tile), :]
            gat_ref[s * tile:(s + 1) * tile, :] = jnp.where(s < live, rows, jnp.zeros_like(rows))
        lhs = jnp.concatenate([tiles_ref[r, s] for s in range(slots)], axis=1)
        out_ref[r] = jnp.dot(lhs, gat_ref[...], preferred_element_type=jnp.float32).astype(out_ref.dtype)


def apply_tiles(tiles, basis, index, counts, rows_per_block=8):
    trows, slots, tile, _ = tiles.shape
    width = basis.shape[-1]
    kernel = functools.partial(_apply_kernel, rows_per_block=rows_per_block, slots=slots, tile=tile)
    spec = pltpu.PrefetchScalarGridSpec(
        num_scalar_prefetch=2,
        grid=(trows // rows_per_block,),
        in_specs=[
            pl.BlockSpec((rows_per_block, slots, tile, tile), lambda i, idx, cnt: (i, 0, 0, 0)),
            pl.BlockSpec(basis.shape, lambda i, idx, cnt: (0, 0)),
        ],
        out_specs=pl.BlockSpec((rows_per_block, tile, width), lambda i, idx, cnt: (i, 0, 0)),
        scratch_shapes=[pltpu.VMEM((slots * tile, width), basis.dtype)],
    )
    return pl.pallas_call(
        kernel,
        grid_spec=spec,
        out_shape=jax.ShapeDtypeStruct((trows, tile, width), jnp.bfloat16),
    )(index.reshape(-1), counts, tiles, basis)


def gather_rows(x, axis):
    n = lax.axis_size(axis)
    got = lax.all_to_all(jnp.broadcast_to(x, (n,) + x.shape), axis, 0, 0, tiled=False)
    return got.reshape((-1,) + x.shape[1:])


def sum_scatter_rows(x, axis):
    n = lax.axis_size(axis)
    got = lax.all_to_all(x.reshape((n, -1) + x.shape[1:]), axis, 0, 0, tiled=False)
    return jnp.sum(got.astype(jnp.float32), axis=0)


def sum_all(x, axes):
    n = 1
    for a in axes:
        n *= lax.axis_size(a)
    piece = jnp.sum(lax.all_to_all(x.reshape(n, -1), axes, 0, 0, tiled=False), axis=0)
    full = lax.all_to_all(jnp.broadcast_to(piece, (n,) + piece.shape), axes, 0, 0, tiled=False)
    return full.reshape(x.shape)


def body(basis, degree_scale, tile_data, tile_index, tile_count):
    tiles = tile_data[:, 0]
    index = tile_index[:, 0]
    counts = tile_count[:, 0]
    rows_dev, width = basis.shape
    tile = tiles.shape[-1]
    nodes = rows_dev * lax.axis_size("row") * lax.axis_size("col")
    scale = degree_scale[:, None]
    probe = (basis.astype(jnp.float32) * scale).astype(jnp.bfloat16)
    number = lax.axis_size("col") * rows_dev // tile

    def one_step(current):
        block_basis = gather_rows(current, "row")
        result = apply_tiles(tiles, block_basis, index, counts)
        summed = sum_scatter_rows(result.reshape(number * tile, width), "col")
        image = summed * scale
        gram = sum_all(gram_of(image, nodes), ("row", "col"))
        return normalize(image, gram)

    def loop_step(i, carry):
        embedding, factor = one_step(carry[0])
        return ((embedding * scale).astype(jnp.bfloat16), embedding, factor)

    start = (probe, jnp.zeros(basis.shape, jnp.float32), jnp.zeros((width, width), jnp.float32))
    _, embedding, factor = lax.fori_loop(0, ITERS, loop_step, start)
    return (embedding, factor)


def solution(mesh):
    placed = (
        P(("row", "col"), None),
        P(("row", "col")),
        P("row", "col", None, None, None),
        P("row", "col", None),
        P("row", "col"),
    )
    return jax.shard_map(
        body, mesh=mesh, in_specs=placed, out_specs=(P(("row", "col"), None), P()), check_vma=False
    )
```

```python
import functools

import jax
import jax.numpy as jnp
from jax import lax
from jax.experimental import pallas as pl
from jax.experimental.pallas import tpu as pltpu
from jax.sharding import PartitionSpec as P

ITERS = 4


def gram_of(image, nodes):
    return (
        lax.dot_general(
            image,
            image,
            (((0,), (0,)), ((), ())),
            precision=lax.Precision.HIGHEST,
            preferred_element_type=jnp.float32,
        )
        / nodes
    )


def dot_hi(a, b):
    return jnp.dot(a, b, precision=lax.Precision.HIGHEST, preferred_element_type=jnp.float32)


def cholesky_and_inverse(g, leaf=128):
    n = g.shape[0]
    if n <= leaf:
        lower = jnp.linalg.cholesky(g)
        eye = jnp.eye(n, dtype=jnp.float32)
        return lower, jax.scipy.linalg.solve_triangular(lower, eye, lower=True)
    h = n // 2
    l11, i11 = cholesky_and_inverse(g[:h, :h], leaf)
    l21 = dot_hi(g[h:, :h], i11.T)
    l22, i22 = cholesky_and_inverse(g[h:, h:] - dot_hi(l21, l21.T), leaf)
    i21 = -dot_hi(i22, dot_hi(l21, i11))
    zero = jnp.zeros((h, n - h), jnp.float32)
    lower = jnp.block([[l11, zero], [l21, l22]])
    inverse = jnp.block([[i11, zero], [i21, i22]])
    return lower, inverse


def _apply_kernel(index_ref, count_ref, tiles_ref, basis_ref, out_ref, gat_ref, *, rows_per_block, slots, tile):
    block = pl.program_id(0)
    for r in range(rows_per_block):
        t = block * rows_per_block + r
        live = count_ref[t]
        for s in range(slots):
            start = pl.multiple_of(index_ref[t * slots + s] * tile, tile)
            rows = basis_ref[pl.ds(start, tile), :]
            gat_ref[s * tile:(s + 1) * tile, :] = jnp.where(s < live, rows, jnp.zeros_like(rows))
        lhs = jnp.concatenate([tiles_ref[r, s] for s in range(slots)], axis=1)
        out_ref[r] = jnp.dot(lhs, gat_ref[...], preferred_element_type=jnp.float32).astype(out_ref.dtype)


def apply_tiles(tiles, basis, index, counts, rows_per_block=8):
    trows, slots, tile, _ = tiles.shape
    width = basis.shape[-1]
    kernel = functools.partial(_apply_kernel, rows_per_block=rows_per_block, slots=slots, tile=tile)
    spec = pltpu.PrefetchScalarGridSpec(
        num_scalar_prefetch=2,
        grid=(trows // rows_per_block,),
        in_specs=[
            pl.BlockSpec((rows_per_block, slots, tile, tile), lambda i, idx, cnt: (i, 0, 0, 0)),
            pl.BlockSpec(basis.shape, lambda i, idx, cnt: (0, 0)),
        ],
        out_specs=pl.BlockSpec((rows_per_block, tile, width), lambda i, idx, cnt: (i, 0, 0)),
        scratch_shapes=[pltpu.VMEM((slots * tile, width), basis.dtype)],
    )
    return pl.pallas_call(
        kernel,
        grid_spec=spec,
        out_shape=jax.ShapeDtypeStruct((trows, tile, width), jnp.bfloat16),
    )(index.reshape(-1), counts, tiles, basis)


def shift_gather(x, axis):
    n = lax.axis_size(axis)
    blocks = [x]
    for d in range(1, n):
        blocks.append(lax.ppermute(x, axis, [(i, (i + d) % n) for i in range(n)]))
    return jnp.concatenate(blocks, axis=0)


def sum_scatter_rows(x, axis):
    n = lax.axis_size(axis)
    got = lax.all_to_all(x.reshape((n, -1) + x.shape[1:]), axis, 0, 0, tiled=False)
    return jnp.sum(got.astype(jnp.float32), axis=0)


def sum_all(x, axes):
    n = 1
    for a in axes:
        n *= lax.axis_size(a)
    piece = jnp.sum(lax.all_to_all(x.reshape(n, -1), axes, 0, 0, tiled=False), axis=0)
    full = lax.all_to_all(jnp.broadcast_to(piece, (n,) + piece.shape), axes, 0, 0, tiled=False)
    return full.reshape(x.shape)


def body(basis, degree_scale, tile_data, tile_index, tile_count):
    tiles = tile_data[:, 0]
    index = tile_index[:, 0]
    counts = tile_count[:, 0]
    rows_dev, width = basis.shape
    tile = tiles.shape[-1]
    nodes = rows_dev * lax.axis_size("row") * lax.axis_size("col")
    scale = degree_scale[:, None]
    probe = (basis.astype(jnp.float32) * scale).astype(jnp.bfloat16)
    number = lax.axis_size("col") * rows_dev // tile
    n_row = lax.axis_size("row")
    per_peer = rows_dev // tile
    me = lax.axis_index("row")
    index = ((me - index // per_peer) % n_row) * per_peer + index % per_peer
    scale_block = shift_gather(scale, "row")

    def loop_step(i, carry):
        block_probe = carry[0]
        result = apply_tiles(tiles, block_probe, index, counts)
        summed = sum_scatter_rows(result.reshape(number * tile, width), "col")
        image = summed * scale
        image_block = shift_gather(image, "row")
        gram = sum_all(gram_of(image, nodes), ("row", "col"))
        gram = (gram + gram.T) * 0.5
        lower, inverse = cholesky_and_inverse(gram)
        embedding = dot_hi(image, inverse.T)
        next_probe = (dot_hi(image_block, inverse.T) * scale_block).astype(jnp.bfloat16)
        return (next_probe, embedding, lower.T)

    start = (shift_gather(probe, "row"), jnp.zeros(basis.shape, jnp.float32), jnp.zeros((width, width), jnp.float32))
    _, embedding, factor = lax.fori_loop(0, ITERS, loop_step, start)
    return (embedding, factor)


def solution(mesh):
    placed = (
        P(("row", "col"), None),
        P(("row", "col")),
        P("row", "col", None, None, None),
        P("row", "col", None),
        P("row", "col"),
    )
    return jax.shard_map(
        body, mesh=mesh, in_specs=placed, out_specs=(P(("row", "col"), None), P()), check_vma=False
    )
```

```python
import functools

import jax
import jax.numpy as jnp
from jax import lax
from jax.experimental import pallas as pl
from jax.experimental.pallas import tpu as pltpu
from jax.sharding import PartitionSpec as P


ITERS = 4


def gram_of(image, nodes):
    return (
        lax.dot_general(
            image,
            image,
            (((0,), (0,)), ((), ())),
            precision=lax.Precision.HIGHEST,
            preferred_element_type=jnp.float32,
        )
        / nodes
    )


def dot_hi(a, b):
    return jnp.dot(a, b, precision=lax.Precision.HIGHEST, preferred_element_type=jnp.float32)


def cholesky_and_inverse(g, leaf=128):
    n = g.shape[0]
    if n <= leaf:
        lower = jnp.linalg.cholesky(g)
        eye = jnp.eye(n, dtype=jnp.float32)
        return lower, jax.scipy.linalg.solve_triangular(lower, eye, lower=True)
    h = n // 2
    l11, i11 = cholesky_and_inverse(g[:h, :h], leaf)
    l21 = dot_hi(g[h:, :h], i11.T)
    l22, i22 = cholesky_and_inverse(g[h:, h:] - dot_hi(l21, l21.T), leaf)
    i21 = -dot_hi(i22, dot_hi(l21, i11))
    zero = jnp.zeros((h, n - h), jnp.float32)
    lower = jnp.block([[l11, zero], [l21, l22]])
    inverse = jnp.block([[i11, zero], [i21, i22]])
    return lower, inverse


def _apply_kernel(index_ref, count_ref, tiles_ref, basis_ref, out_ref, gat_ref, *, rows_per_block, slots, tile):
    block = pl.program_id(0)
    for r in range(rows_per_block):
        t = block * rows_per_block + r
        live = count_ref[t]
        for s in range(slots):
            start = pl.multiple_of(index_ref[t * slots + s] * tile, tile)
            rows = basis_ref[pl.ds(start, tile), :]
            gat_ref[s * tile:(s + 1) * tile, :] = jnp.where(s < live, rows, jnp.zeros_like(rows))
        lhs = jnp.concatenate([tiles_ref[r, s] for s in range(slots)], axis=1)
        out_ref[r] = jnp.dot(lhs, gat_ref[...], preferred_element_type=jnp.float32).astype(out_ref.dtype)


def apply_tiles(tiles, basis, index, counts, rows_per_block=8):
    trows, slots, tile, _ = tiles.shape
    width = basis.shape[-1]
    kernel = functools.partial(_apply_kernel, rows_per_block=rows_per_block, slots=slots, tile=tile)
    spec = pltpu.PrefetchScalarGridSpec(
        num_scalar_prefetch=2,
        grid=(trows // rows_per_block,),
        in_specs=[
            pl.BlockSpec((rows_per_block, slots, tile, tile), lambda i, idx, cnt: (i, 0, 0, 0)),
            pl.BlockSpec(basis.shape, lambda i, idx, cnt: (0, 0)),
        ],
        out_specs=pl.BlockSpec((rows_per_block, tile, width), lambda i, idx, cnt: (i, 0, 0)),
        scratch_shapes=[pltpu.VMEM((slots * tile, width), basis.dtype)],
    )
    return pl.pallas_call(
        kernel,
        grid_spec=spec,
        out_shape=jax.ShapeDtypeStruct((trows, tile, width), jnp.bfloat16),
    )(index.reshape(-1), counts, tiles, basis)


def sum_scatter_rows(x, axis):
    n = lax.axis_size(axis)
    got = lax.all_to_all(x.reshape((n, -1) + x.shape[1:]), axis, 0, 0, tiled=False)
    return jnp.sum(got.astype(jnp.float32), axis=0)


def sum_all(x, axes):
    n = 1
    for a in axes:
        n *= lax.axis_size(a)
    piece = jnp.sum(lax.all_to_all(x.reshape(n, -1), axes, 0, 0, tiled=False), axis=0)
    full = lax.all_to_all(jnp.broadcast_to(piece, (n,) + piece.shape), axes, 0, 0, tiled=False)
    return full.reshape(x.shape)


def body(basis, degree_scale, tile_data, tile_index, tile_count):
    tiles = tile_data[:, 0]
    index = tile_index[:, 0]
    counts = tile_count[:, 0]
    rows_dev, width = basis.shape
    tile = tiles.shape[-1]
    nodes = rows_dev * lax.axis_size("row") * lax.axis_size("col")
    scale = degree_scale[:, None]
    probe = (basis.astype(jnp.float32) * scale).astype(jnp.bfloat16)
    number = lax.axis_size("col") * rows_dev // tile
    scale_block = lax.all_gather(scale, "row", axis=0, tiled=True)

    def loop_step(i, carry):
        block_probe = carry[0]
        result = apply_tiles(tiles, block_probe, index, counts)
        summed = sum_scatter_rows(result.reshape(number * tile, width), "col")
        image = summed * scale
        image_block = lax.all_gather(image, "row", axis=0, tiled=True)
        gram = sum_all(gram_of(image, nodes), ("row", "col"))
        gram = (gram + gram.T) * 0.5
        lower, inverse = cholesky_and_inverse(gram)
        embedding = dot_hi(image, inverse.T)
        next_probe = (dot_hi(image_block, inverse.T) * scale_block).astype(jnp.bfloat16)
        return (next_probe, embedding, lower.T)

    start = (lax.all_gather(probe, "row", axis=0, tiled=True), jnp.zeros(basis.shape, jnp.float32), jnp.zeros((width, width), jnp.float32))
    _, embedding, factor = lax.fori_loop(0, ITERS, loop_step, start)
    return (embedding, factor)


def solution(mesh):
    placed = (
        P(("row", "col"), None),
        P(("row", "col")),
        P("row", "col", None, None, None),
        P("row", "col", None),
        P("row", "col"),
    )
    return jax.shard_map(
        body, mesh=mesh, in_specs=placed, out_specs=(P(("row", "col"), None), P()), check_vma=False
    )
```

```python
import functools

import jax
import jax.numpy as jnp
from jax import lax
from jax.experimental import pallas as pl
from jax.experimental.pallas import tpu as pltpu
from jax.sharding import PartitionSpec as P


ITERS = 4


def gram_of(image, nodes):
    return (
        lax.dot_general(
            image,
            image,
            (((0,), (0,)), ((), ())),
            precision=lax.Precision.HIGHEST,
            preferred_element_type=jnp.float32,
        )
        / nodes
    )


def dot_hi(a, b):
    return jnp.dot(a, b, precision=lax.Precision.HIGHEST, preferred_element_type=jnp.float32)


def cholesky_and_inverse(g, leaf=128):
    n = g.shape[0]
    if n <= leaf:
        lower = jnp.linalg.cholesky(g)
        eye = jnp.eye(n, dtype=jnp.float32)
        return lower, jax.scipy.linalg.solve_triangular(lower, eye, lower=True)
    h = n // 2
    l11, i11 = cholesky_and_inverse(g[:h, :h], leaf)
    l21 = dot_hi(g[h:, :h], i11.T)
    l22, i22 = cholesky_and_inverse(g[h:, h:] - dot_hi(l21, l21.T), leaf)
    i21 = -dot_hi(i22, dot_hi(l21, i11))
    zero = jnp.zeros((h, n - h), jnp.float32)
    lower = jnp.block([[l11, zero], [l21, l22]])
    inverse = jnp.block([[i11, zero], [i21, i22]])
    return lower, inverse


def _apply_kernel(index_ref, count_ref, tiles_ref, basis_ref, out_ref, gat_ref, *, rows_per_block, slots, tile):
    block = pl.program_id(0)
    for r in range(rows_per_block):
        t = block * rows_per_block + r
        live = count_ref[t]
        for s in range(slots):
            start = pl.multiple_of(index_ref[t * slots + s] * tile, tile)
            rows = basis_ref[pl.ds(start, tile), :]
            gat_ref[s * tile:(s + 1) * tile, :] = jnp.where(s < live, rows, jnp.zeros_like(rows))
        lhs = jnp.concatenate([tiles_ref[r, s] for s in range(slots)], axis=1)
        out_ref[r] = jnp.dot(lhs, gat_ref[...], preferred_element_type=jnp.float32).astype(out_ref.dtype)


def apply_tiles(tiles, basis, index, counts, rows_per_block=8):
    trows, slots, tile, _ = tiles.shape
    width = basis.shape[-1]
    kernel = functools.partial(_apply_kernel, rows_per_block=rows_per_block, slots=slots, tile=tile)
    spec = pltpu.PrefetchScalarGridSpec(
        num_scalar_prefetch=2,
        grid=(trows // rows_per_block,),
        in_specs=[
            pl.BlockSpec((rows_per_block, slots, tile, tile), lambda i, idx, cnt: (i, 0, 0, 0)),
            pl.BlockSpec(basis.shape, lambda i, idx, cnt: (0, 0)),
        ],
        out_specs=pl.BlockSpec((rows_per_block, tile, width), lambda i, idx, cnt: (i, 0, 0)),
        scratch_shapes=[pltpu.VMEM((slots * tile, width), basis.dtype)],
    )
    return pl.pallas_call(
        kernel,
        grid_spec=spec,
        out_shape=jax.ShapeDtypeStruct((trows, tile, width), jnp.bfloat16),
    )(index.reshape(-1), counts, tiles, basis)


def gather_rows(x, axis):
    n = lax.axis_size(axis)
    got = lax.all_to_all(jnp.broadcast_to(x, (n,) + x.shape), axis, 0, 0, tiled=False)
    return got.reshape((-1,) + x.shape[1:])


def sum_scatter_rows(x, axis):
    n = lax.axis_size(axis)
    got = lax.all_to_all(x.reshape((n, -1) + x.shape[1:]), axis, 0, 0, tiled=False)
    return jnp.sum(got.astype(jnp.float32), axis=0)


def sum_all(x, axes):
    n = 1
    for a in axes:
        n *= lax.axis_size(a)
    piece = jnp.sum(lax.all_to_all(x.reshape(n, -1), axes, 0, 0, tiled=False), axis=0)
    full = lax.all_to_all(jnp.broadcast_to(piece, (n,) + piece.shape), axes, 0, 0, tiled=False)
    return full.reshape(x.shape)


def body(basis, degree_scale, tile_data, tile_index, tile_count):
    tiles = tile_data[:, 0]
    index = tile_index[:, 0]
    counts = tile_count[:, 0]
    rows_dev, width = basis.shape
    tile = tiles.shape[-1]
    nodes = rows_dev * lax.axis_size("row") * lax.axis_size("col")
    scale = degree_scale[:, None]
    probe = (basis.astype(jnp.float32) * scale).astype(jnp.bfloat16)
    number = lax.axis_size("col") * rows_dev // tile
    scale_block = gather_rows(degree_scale, "row")[:, None]

    def loop_step(i, carry):
        block_probe = carry[0]
        result = apply_tiles(tiles, block_probe, index, counts)
        summed = sum_scatter_rows(result.reshape(number * tile, width), "col")
        image = summed * scale
        gram = sum_all(gram_of(image, nodes), ("row", "col"))
        image_late, gram = lax.optimization_barrier((image, gram))
        image_block = lax.all_gather(image_late, "row", axis=0, tiled=True)
        gram = (gram + gram.T) * 0.5
        lower, inverse = cholesky_and_inverse(gram)
        embedding = dot_hi(image, inverse.T)
        next_probe = (dot_hi(image_block, inverse.T) * scale_block).astype(jnp.bfloat16)
        return (next_probe, embedding, lower.T)

    start = (gather_rows(probe, "row"), jnp.zeros(basis.shape, jnp.float32), jnp.zeros((width, width), jnp.float32))
    _, embedding, factor = lax.fori_loop(0, ITERS, loop_step, start)
    return (embedding, factor)


def solution(mesh):
    placed = (
        P(("row", "col"), None),
        P(("row", "col")),
        P("row", "col", None, None, None),
        P("row", "col", None),
        P("row", "col"),
    )
    return jax.shard_map(
        body, mesh=mesh, in_specs=placed, out_specs=(P(("row", "col"), None), P()), check_vma=False
    )
```

```python
import functools

import jax
import jax.numpy as jnp
from jax import lax
from jax.experimental import pallas as pl
from jax.experimental.pallas import tpu as pltpu
from jax.sharding import PartitionSpec as P


ITERS = 4


def gram_of(image, nodes):
    return (
        lax.dot_general(
            image,
            image,
            (((0,), (0,)), ((), ())),
            precision=lax.Precision.HIGHEST,
            preferred_element_type=jnp.float32,
        )
        / nodes
    )


def dot_hi(a, b):
    return jnp.dot(a, b, precision=lax.Precision.HIGHEST, preferred_element_type=jnp.float32)


def cholesky_and_inverse(g, leaf=128):
    n = g.shape[0]
    if n <= leaf:
        lower = jnp.linalg.cholesky(g)
        eye = jnp.eye(n, dtype=jnp.float32)
        return lower, jax.scipy.linalg.solve_triangular(lower, eye, lower=True)
    h = n // 2
    l11, i11 = cholesky_and_inverse(g[:h, :h], leaf)
    l21 = dot_hi(g[h:, :h], i11.T)
    l22, i22 = cholesky_and_inverse(g[h:, h:] - dot_hi(l21, l21.T), leaf)
    i21 = -dot_hi(i22, dot_hi(l21, i11))
    zero = jnp.zeros((h, n - h), jnp.float32)
    lower = jnp.block([[l11, zero], [l21, l22]])
    inverse = jnp.block([[i11, zero], [i21, i22]])
    return lower, inverse


def _apply_kernel(index_ref, count_ref, tiles_ref, basis_ref, out_ref, gat_ref, *, rows_per_block, slots, tile):
    block = pl.program_id(0)
    for r in range(rows_per_block):
        t = block * rows_per_block + r
        live = count_ref[t]
        for s in range(slots):
            start = pl.multiple_of(index_ref[t * slots + s] * tile, tile)
            rows = basis_ref[pl.ds(start, tile), :]
            gat_ref[s * tile:(s + 1) * tile, :] = jnp.where(s < live, rows, jnp.zeros_like(rows))
        lhs = jnp.concatenate([tiles_ref[r, s] for s in range(slots)], axis=1)
        out_ref[r] = jnp.dot(lhs, gat_ref[...], preferred_element_type=jnp.float32).astype(out_ref.dtype)


def apply_tiles(tiles, basis, index, counts, rows_per_block=8):
    trows, slots, tile, _ = tiles.shape
    width = basis.shape[-1]
    kernel = functools.partial(_apply_kernel, rows_per_block=rows_per_block, slots=slots, tile=tile)
    spec = pltpu.PrefetchScalarGridSpec(
        num_scalar_prefetch=2,
        grid=(trows // rows_per_block,),
        in_specs=[
            pl.BlockSpec((rows_per_block, slots, tile, tile), lambda i, idx, cnt: (i, 0, 0, 0)),
            pl.BlockSpec(basis.shape, lambda i, idx, cnt: (0, 0)),
        ],
        out_specs=pl.BlockSpec((rows_per_block, tile, width), lambda i, idx, cnt: (i, 0, 0)),
        scratch_shapes=[pltpu.VMEM((slots * tile, width), basis.dtype)],
    )
    return pl.pallas_call(
        kernel,
        grid_spec=spec,
        out_shape=jax.ShapeDtypeStruct((trows, tile, width), jnp.bfloat16),
    )(index.reshape(-1), counts, tiles, basis)


def gather_rows(x, axis):
    n = lax.axis_size(axis)
    got = lax.all_to_all(jnp.broadcast_to(x, (n,) + x.shape), axis, 0, 0, tiled=False)
    return got.reshape((-1,) + x.shape[1:])


def sum_scatter_rows(x, axis):
    n = lax.axis_size(axis)
    got = lax.all_to_all(x.reshape((n, -1) + x.shape[1:]), axis, 0, 0, tiled=False)
    return jnp.sum(got.astype(jnp.float32), axis=0)


def sum_all(x, axes):
    n = 1
    for a in axes:
        n *= lax.axis_size(a)
    piece = jnp.sum(lax.all_to_all(x.reshape(n, -1), axes, 0, 0, tiled=False), axis=0)
    full = lax.all_to_all(jnp.broadcast_to(piece, (n,) + piece.shape), axes, 0, 0, tiled=False)
    return full.reshape(x.shape)


def body(basis, degree_scale, tile_data, tile_index, tile_count):
    tiles = tile_data[:, 0]
    index = tile_index[:, 0]
    counts = tile_count[:, 0]
    rows_dev, width = basis.shape
    tile = tiles.shape[-1]
    nodes = rows_dev * lax.axis_size("row") * lax.axis_size("col")
    scale = degree_scale[:, None]
    probe = (basis.astype(jnp.float32) * scale).astype(jnp.bfloat16)
    number = lax.axis_size("col") * rows_dev // tile
    scale_block = gather_rows(degree_scale, "row")[:, None]

    def loop_step(i, carry):
        block_probe = carry[0]
        result = apply_tiles(tiles, block_probe, index, counts)
        summed = sum_scatter_rows(result.reshape(number * tile, width), "col")
        image = summed * scale
        gram = sum_all(gram_of(image, nodes), ("row", "col"))
        image_late, gram = lax.optimization_barrier((image, gram))
        image_block = lax.all_gather(image_late, "row", axis=0, tiled=True)
        gram = (gram + gram.T) * 0.5
        lower, inverse = cholesky_and_inverse(gram)
        next_probe = (dot_hi(image_block, inverse.T) * scale_block).astype(jnp.bfloat16)
        return (next_probe, image, inverse, lower)

    square = jnp.zeros((width, width), jnp.float32)
    start = (gather_rows(probe, "row"), jnp.zeros(basis.shape, jnp.float32), square, square)
    _, image, inverse, lower = lax.fori_loop(0, ITERS, loop_step, start)
    embedding = dot_hi(image, inverse.T)
    factor = lower.T
    return (embedding, factor)


def solution(mesh):
    placed = (
        P(("row", "col"), None),
        P(("row", "col")),
        P("row", "col", None, None, None),
        P("row", "col", None),
        P("row", "col"),
    )
    return jax.shard_map(
        body, mesh=mesh, in_specs=placed, out_specs=(P(("row", "col"), None), P()), check_vma=False
    )
```

```python
import functools

import jax
import jax.numpy as jnp
from jax import lax
from jax.experimental import pallas as pl
from jax.experimental.pallas import tpu as pltpu
from jax.sharding import PartitionSpec as P


ITERS = 4


def gram_of(image, nodes):
    return (
        lax.dot_general(
            image,
            image,
            (((0,), (0,)), ((), ())),
            precision=lax.Precision.HIGHEST,
            preferred_element_type=jnp.float32,
        )
        / nodes
    )


def dot_hi(a, b):
    return jnp.dot(a, b, precision=lax.Precision.HIGHEST, preferred_element_type=jnp.float32)


def cholesky_and_inverse(g, leaf=128):
    n = g.shape[0]
    if n <= leaf:
        lower = jnp.linalg.cholesky(g)
        eye = jnp.eye(n, dtype=jnp.float32)
        return lower, jax.scipy.linalg.solve_triangular(lower, eye, lower=True)
    h = n // 2
    l11, i11 = cholesky_and_inverse(g[:h, :h], leaf)
    l21 = dot_hi(g[h:, :h], i11.T)
    l22, i22 = cholesky_and_inverse(g[h:, h:] - dot_hi(l21, l21.T), leaf)
    i21 = -dot_hi(i22, dot_hi(l21, i11))
    zero = jnp.zeros((h, n - h), jnp.float32)
    lower = jnp.block([[l11, zero], [l21, l22]])
    inverse = jnp.block([[i11, zero], [i21, i22]])
    return lower, inverse


def _apply_kernel(index_ref, count_ref, tiles_ref, basis_ref, out_ref, gat_ref, *, rows_per_block, slots, tile):
    block = pl.program_id(0)
    for r in range(rows_per_block):
        t = block * rows_per_block + r
        live = count_ref[t]
        for s in range(slots):
            start = pl.multiple_of(index_ref[t * slots + s] * tile, tile)
            rows = basis_ref[pl.ds(start, tile), :]
            gat_ref[s * tile:(s + 1) * tile, :] = jnp.where(s < live, rows, jnp.zeros_like(rows))
        lhs = jnp.concatenate([tiles_ref[r, s] for s in range(slots)], axis=1)
        out_ref[r] = jnp.dot(lhs, gat_ref[...], preferred_element_type=jnp.float32).astype(out_ref.dtype)


def apply_tiles(tiles, basis, index, counts, rows_per_block=16):
    trows, slots, tile, _ = tiles.shape
    width = basis.shape[-1]
    kernel = functools.partial(_apply_kernel, rows_per_block=rows_per_block, slots=slots, tile=tile)
    spec = pltpu.PrefetchScalarGridSpec(
        num_scalar_prefetch=2,
        grid=(trows // rows_per_block,),
        in_specs=[
            pl.BlockSpec((rows_per_block, slots, tile, tile), lambda i, idx, cnt: (i, 0, 0, 0)),
            pl.BlockSpec(basis.shape, lambda i, idx, cnt: (0, 0)),
        ],
        out_specs=pl.BlockSpec((rows_per_block, tile, width), lambda i, idx, cnt: (i, 0, 0)),
        scratch_shapes=[pltpu.VMEM((slots * tile, width), basis.dtype)],
    )
    return pl.pallas_call(
        kernel,
        grid_spec=spec,
        out_shape=jax.ShapeDtypeStruct((trows, tile, width), jnp.bfloat16),
    )(index.reshape(-1), counts, tiles, basis)


def gather_rows(x, axis):
    n = lax.axis_size(axis)
    got = lax.all_to_all(jnp.broadcast_to(x, (n,) + x.shape), axis, 0, 0, tiled=False)
    return got.reshape((-1,) + x.shape[1:])


def sum_scatter_rows(x, axis):
    n = lax.axis_size(axis)
    got = lax.all_to_all(x.reshape((n, -1) + x.shape[1:]), axis, 0, 0, tiled=False)
    return jnp.sum(got.astype(jnp.float32), axis=0)


def sum_all(x, axes):
    n = 1
    for a in axes:
        n *= lax.axis_size(a)
    piece = jnp.sum(lax.all_to_all(x.reshape(n, -1), axes, 0, 0, tiled=False), axis=0)
    full = lax.all_to_all(jnp.broadcast_to(piece, (n,) + piece.shape), axes, 0, 0, tiled=False)
    return full.reshape(x.shape)


def body(basis, degree_scale, tile_data, tile_index, tile_count):
    tiles = tile_data[:, 0]
    index = tile_index[:, 0]
    counts = tile_count[:, 0]
    rows_dev, width = basis.shape
    tile = tiles.shape[-1]
    nodes = rows_dev * lax.axis_size("row") * lax.axis_size("col")
    scale = degree_scale[:, None]
    probe = (basis.astype(jnp.float32) * scale).astype(jnp.bfloat16)
    number = lax.axis_size("col") * rows_dev // tile
    scale_block = gather_rows(degree_scale, "row")[:, None]

    def loop_step(i, carry):
        block_probe = carry[0]
        result = apply_tiles(tiles, block_probe, index, counts)
        summed = sum_scatter_rows(result.reshape(number * tile, width), "col")
        image = summed * scale
        gram = sum_all(gram_of(image, nodes), ("row", "col"))
        image_late, gram = lax.optimization_barrier((image, gram))
        image_block = lax.all_gather(image_late, "row", axis=0, tiled=True)
        gram = (gram + gram.T) * 0.5
        lower, inverse = cholesky_and_inverse(gram)
        normalized = jnp.dot(image_block, inverse.T, precision=lax.Precision.HIGH, preferred_element_type=jnp.float32)
        next_probe = (normalized * scale_block).astype(jnp.bfloat16)
        return (next_probe, image, inverse, lower)

    square = jnp.zeros((width, width), jnp.float32)
    start = (gather_rows(probe, "row"), jnp.zeros(basis.shape, jnp.float32), square, square)
    _, image, inverse, lower = lax.fori_loop(0, ITERS, loop_step, start)
    embedding = dot_hi(image, inverse.T)
    factor = lower.T
    return (embedding, factor)


def solution(mesh):
    placed = (
        P(("row", "col"), None),
        P(("row", "col")),
        P("row", "col", None, None, None),
        P("row", "col", None),
        P("row", "col"),
    )
    return jax.shard_map(
        body, mesh=mesh, in_specs=placed, out_specs=(P(("row", "col"), None), P()), check_vma=False
    )
```

```python
import functools

import jax
import jax.numpy as jnp
from jax import lax
from jax.experimental import pallas as pl
from jax.experimental.pallas import tpu as pltpu
from jax.sharding import PartitionSpec as P


ITERS = 4
SC_ROWS = 64


def gram_of(image, nodes):
    return (
        lax.dot_general(
            image,
            image,
            (((0,), (0,)), ((), ())),
            precision=lax.Precision.HIGHEST,
            preferred_element_type=jnp.float32,
        )
        / nodes
    )


def dot_hi(a, b):
    return jnp.dot(a, b, precision=lax.Precision.HIGHEST, preferred_element_type=jnp.float32)


def cholesky_and_inverse(g, leaf=128):
    n = g.shape[0]
    if n <= leaf:
        lower = jnp.linalg.cholesky(g)
        eye = jnp.eye(n, dtype=jnp.float32)
        return lower, jax.scipy.linalg.solve_triangular(lower, eye, lower=True)
    h = n // 2
    l11, i11 = cholesky_and_inverse(g[:h, :h], leaf)
    l21 = dot_hi(g[h:, :h], i11.T)
    l22, i22 = cholesky_and_inverse(g[h:, h:] - dot_hi(l21, l21.T), leaf)
    i21 = -dot_hi(i22, dot_hi(l21, i11))
    zero = jnp.zeros((h, n - h), jnp.float32)
    lower = jnp.block([[l11, zero], [l21, l22]])
    inverse = jnp.block([[i11, zero], [i21, i22]])
    return lower, inverse


def _apply_kernel(index_ref, count_ref, tiles_ref, basis_ref, out_ref, gat_ref, *, rows_per_block, slots, tile):
    block = pl.program_id(0)
    for r in range(rows_per_block):
        t = block * rows_per_block + r
        live = count_ref[t]
        for s in range(slots):
            start = pl.multiple_of(index_ref[t * slots + s] * tile, tile)
            rows = basis_ref[pl.ds(start, tile), :]
            gat_ref[s * tile:(s + 1) * tile, :] = jnp.where(s < live, rows, jnp.zeros_like(rows))
        lhs = jnp.concatenate([tiles_ref[r, s] for s in range(slots)], axis=1)
        out_ref[r] = jnp.dot(lhs, gat_ref[...], preferred_element_type=jnp.float32).astype(out_ref.dtype)


def apply_tiles(tiles, basis, index, counts, rows_per_block=16):
    trows, slots, tile, _ = tiles.shape
    width = basis.shape[-1]
    kernel = functools.partial(_apply_kernel, rows_per_block=rows_per_block, slots=slots, tile=tile)
    spec = pltpu.PrefetchScalarGridSpec(
        num_scalar_prefetch=2,
        grid=(trows // rows_per_block,),
        in_specs=[
            pl.BlockSpec((rows_per_block, slots, tile, tile), lambda i, idx, cnt: (i, 0, 0, 0)),
            pl.BlockSpec(basis.shape, lambda i, idx, cnt: (0, 0)),
        ],
        out_specs=pl.BlockSpec((rows_per_block, tile, width), lambda i, idx, cnt: (i, 0, 0)),
        scratch_shapes=[pltpu.VMEM((slots * tile, width), basis.dtype)],
    )
    return pl.pallas_call(
        kernel,
        grid_spec=spec,
        out_shape=jax.ShapeDtypeStruct((trows, tile, width), jnp.bfloat16),
    )(index.reshape(-1), counts, tiles, basis)


def gather_rows(x, axis):
    n = lax.axis_size(axis)
    got = lax.all_to_all(jnp.broadcast_to(x, (n,) + x.shape), axis, 0, 0, tiled=False)
    return got.reshape((-1,) + x.shape[1:])


def sum_scatter_rows(x, axis):
    n = lax.axis_size(axis)
    got = lax.all_to_all(x.reshape((n, -1) + x.shape[1:]), axis, 0, 0, tiled=False)
    return jnp.sum(got.astype(jnp.float32), axis=0)


def sum_all(x, axes):
    n = 1
    for a in axes:
        n *= lax.axis_size(a)
    piece = jnp.sum(lax.all_to_all(x.reshape(n, -1), axes, 0, 0, tiled=False), axis=0)
    full = lax.all_to_all(jnp.broadcast_to(piece, (n,) + piece.shape), axes, 0, 0, tiled=False)
    return full.reshape(x.shape)


def body(basis, degree_scale, tile_data, tile_index, tile_count):
    tiles = tile_data[:, 0]
    index = tile_index[:, 0]
    counts = tile_count[:, 0]
    rows_dev, width = basis.shape
    nodes = rows_dev * lax.axis_size("row") * lax.axis_size("col")
    scale = degree_scale[:, None]
    probe = (basis.astype(jnp.float32) * scale).astype(jnp.bfloat16)
    n_col = lax.axis_size("col")
    scale_block = lax.all_gather(degree_scale, "row", axis=0, tiled=True)[:, None]

    def loop_step(i, carry):
        block_probe = carry[0]
        result = apply_tiles(tiles, block_probe, index, counts)
        parts = result.reshape(n_col, -1, width)
        head = lax.psum_scatter(
            parts[:, :SC_ROWS].reshape(-1, width), "col", scatter_dimension=0, tiled=True
        ).astype(jnp.float32)
        rest = sum_scatter_rows(parts[:, SC_ROWS:].reshape(-1, width), "col")
        summed = jnp.concatenate([head, rest], axis=0)
        image = summed * scale
        gram = sum_all(gram_of(image, nodes), ("row", "col"))
        image_late, gram = lax.optimization_barrier((image, gram))
        image_block = lax.all_gather(image_late, "row", axis=0, tiled=True)
        gram = (gram + gram.T) * 0.5
        lower, inverse = cholesky_and_inverse(gram)
        normalized = jnp.dot(image_block, inverse.T, precision=lax.Precision.HIGH, preferred_element_type=jnp.float32)
        next_probe = (normalized * scale_block).astype(jnp.bfloat16)
        return (next_probe, image, inverse, lower)

    square = jnp.zeros((width, width), jnp.float32)
    start = (gather_rows(probe, "row"), jnp.zeros(basis.shape, jnp.float32), square, square)
    _, image, inverse, lower = lax.fori_loop(0, ITERS, loop_step, start)
    embedding = dot_hi(image, inverse.T)
    factor = lower.T
    return (embedding, factor)


def solution(mesh):
    placed = (
        P(("row", "col"), None),
        P(("row", "col")),
        P("row", "col", None, None, None),
        P("row", "col", None),
        P("row", "col"),
    )
    return jax.shard_map(
        body, mesh=mesh, in_specs=placed, out_specs=(P(("row", "col"), None), P()), check_vma=False
    )
```

```python
import functools

import jax
import jax.numpy as jnp
from jax import lax
from jax.experimental import pallas as pl
from jax.experimental.pallas import tpu as pltpu
from jax.sharding import PartitionSpec as P


ITERS = 4


def gram_of(image, nodes):
    return (
        lax.dot_general(
            image,
            image,
            (((0,), (0,)), ((), ())),
            precision=lax.Precision.HIGHEST,
            preferred_element_type=jnp.float32,
        )
        / nodes
    )


def dot_hi(a, b):
    return jnp.dot(a, b, precision=lax.Precision.HIGHEST, preferred_element_type=jnp.float32)


def cholesky_and_inverse(g, leaf=128):
    n = g.shape[0]
    if n <= leaf:
        lower = jnp.linalg.cholesky(g)
        eye = jnp.eye(n, dtype=jnp.float32)
        return lower, jax.scipy.linalg.solve_triangular(lower, eye, lower=True)
    h = n // 2
    l11, i11 = cholesky_and_inverse(g[:h, :h], leaf)
    l21 = dot_hi(g[h:, :h], i11.T)
    l22, i22 = cholesky_and_inverse(g[h:, h:] - dot_hi(l21, l21.T), leaf)
    i21 = -dot_hi(i22, dot_hi(l21, i11))
    zero = jnp.zeros((h, n - h), jnp.float32)
    lower = jnp.block([[l11, zero], [l21, l22]])
    inverse = jnp.block([[i11, zero], [i21, i22]])
    return lower, inverse


def _apply_kernel(index_ref, count_ref, tiles_ref, basis_ref, out_ref, gat_ref, *, rows_per_block, slots, tile):
    block = pl.program_id(0)
    for r in range(rows_per_block):
        t = block * rows_per_block + r
        live = count_ref[t]
        for s in range(slots):
            start = pl.multiple_of(index_ref[t * slots + s] * tile, tile)
            rows = basis_ref[pl.ds(start, tile), :]
            gat_ref[s * tile:(s + 1) * tile, :] = jnp.where(s < live, rows, jnp.zeros_like(rows))
        lhs = jnp.concatenate([tiles_ref[r, 0, s] for s in range(slots)], axis=1)
        out_ref[r] = jnp.dot(lhs, gat_ref[...], preferred_element_type=jnp.float32).astype(out_ref.dtype)


def apply_tiles(tiles, basis, index, counts, half, rows_per_block=8):
    trows, slots, tile, _ = tiles.shape
    width = basis.shape[-1]
    pairs = tiles.reshape(trows // 2, 2, slots, tile, tile)
    index = index.reshape(trows // 2, 2, slots)[:, half].reshape(-1)
    counts = counts.reshape(trows // 2, 2)[:, half]
    kernel = functools.partial(_apply_kernel, rows_per_block=rows_per_block, slots=slots, tile=tile)
    spec = pltpu.PrefetchScalarGridSpec(
        num_scalar_prefetch=2,
        grid=(trows // 2 // rows_per_block,),
        in_specs=[
            pl.BlockSpec((rows_per_block, 1, slots, tile, tile), lambda i, idx, cnt: (i, half, 0, 0, 0)),
            pl.BlockSpec(basis.shape, lambda i, idx, cnt: (0, 0)),
        ],
        out_specs=pl.BlockSpec((rows_per_block, tile, width), lambda i, idx, cnt: (i, 0, 0)),
        scratch_shapes=[pltpu.VMEM((slots * tile, width), basis.dtype)],
    )
    return pl.pallas_call(
        kernel,
        grid_spec=spec,
        out_shape=jax.ShapeDtypeStruct((trows // 2, tile, width), jnp.bfloat16),
    )(index, counts, pairs, basis)


def gather_rows(x, axis):
    n = lax.axis_size(axis)
    got = lax.all_to_all(jnp.broadcast_to(x, (n,) + x.shape), axis, 0, 0, tiled=False)
    return got.reshape((-1,) + x.shape[1:])


def sum_scatter_rows(x, axis):
    n = lax.axis_size(axis)
    got = lax.all_to_all(x.reshape((n, -1) + x.shape[1:]), axis, 0, 0, tiled=False)
    return jnp.sum(got.astype(jnp.float32), axis=0)


def sum_all(x, axes):
    n = 1
    for a in axes:
        n *= lax.axis_size(a)
    piece = jnp.sum(lax.all_to_all(x.reshape(n, -1), axes, 0, 0, tiled=False), axis=0)
    full = lax.all_to_all(jnp.broadcast_to(piece, (n,) + piece.shape), axes, 0, 0, tiled=False)
    return full.reshape(x.shape)


def body(basis, degree_scale, tile_data, tile_index, tile_count):
    tiles = tile_data[:, 0]
    index = tile_index[:, 0]
    counts = tile_count[:, 0]
    rows_dev, width = basis.shape
    nodes = rows_dev * lax.axis_size("row") * lax.axis_size("col")
    scale = degree_scale[:, None]
    probe = (basis.astype(jnp.float32) * scale).astype(jnp.bfloat16)
    scale_block = lax.all_gather(degree_scale, "row", axis=0, tiled=True)[:, None]

    def loop_step(i, carry):
        block_probe = carry[0]
        first = sum_scatter_rows(apply_tiles(tiles, block_probe, index, counts, 0).reshape(-1, width), "col")
        second = sum_scatter_rows(apply_tiles(tiles, block_probe, index, counts, 1).reshape(-1, width), "col")
        summed = jnp.concatenate([first, second], axis=0)
        image = summed * scale
        gram = sum_all(gram_of(image, nodes), ("row", "col"))
        image_late, gram = lax.optimization_barrier((image, gram))
        image_block = lax.all_gather(image_late, "row", axis=0, tiled=True)
        gram = (gram + gram.T) * 0.5
        lower, inverse = cholesky_and_inverse(gram)
        normalized = jnp.dot(image_block, inverse.T, precision=lax.Precision.HIGH, preferred_element_type=jnp.float32)
        next_probe = (normalized * scale_block).astype(jnp.bfloat16)
        return (next_probe, image, inverse, lower)

    square = jnp.zeros((width, width), jnp.float32)
    start = (gather_rows(probe, "row"), jnp.zeros(basis.shape, jnp.float32), square, square)
    _, image, inverse, lower = lax.fori_loop(0, ITERS, loop_step, start)
    embedding = dot_hi(image, inverse.T)
    factor = lower.T
    return (embedding, factor)


def solution(mesh):
    placed = (
        P(("row", "col"), None),
        P(("row", "col")),
        P("row", "col", None, None, None),
        P("row", "col", None),
        P("row", "col"),
    )
    return jax.shard_map(
        body, mesh=mesh, in_specs=placed, out_specs=(P(("row", "col"), None), P()), check_vma=False
    )
```

```python
import functools

import jax
import jax.numpy as jnp
from jax import lax
from jax.experimental import pallas as pl
from jax.experimental.pallas import tpu as pltpu
from jax.sharding import PartitionSpec as P


ITERS = 4


def gram_of(image, nodes):
    return (
        lax.dot_general(
            image,
            image,
            (((0,), (0,)), ((), ())),
            precision=lax.Precision.HIGHEST,
            preferred_element_type=jnp.float32,
        )
        / nodes
    )


def dot_hi(a, b):
    return jnp.dot(a, b, precision=lax.Precision.HIGHEST, preferred_element_type=jnp.float32)


def cholesky_and_inverse(g, leaf=128):
    n = g.shape[0]
    if n <= leaf:
        lower = jnp.linalg.cholesky(g, symmetrize_input=False)
        eye = jnp.eye(n, dtype=jnp.float32)
        return lower, jax.scipy.linalg.solve_triangular(lower, eye, lower=True)
    h = n // 2
    l11, i11 = cholesky_and_inverse(g[:h, :h], leaf)
    l21 = dot_hi(g[h:, :h], i11.T)
    l22, i22 = cholesky_and_inverse(g[h:, h:] - dot_hi(l21, l21.T), leaf)
    i21 = -dot_hi(i22, dot_hi(l21, i11))
    zero = jnp.zeros((h, n - h), jnp.float32)
    lower = jnp.block([[l11, zero], [l21, l22]])
    inverse = jnp.block([[i11, zero], [i21, i22]])
    return lower, inverse


def _apply_kernel(index_ref, count_ref, tiles_ref, basis_ref, out_ref, gat_ref, *, rows_per_block, slots, tile):
    block = pl.program_id(0)
    for r in range(rows_per_block):
        t = block * rows_per_block + r
        live = count_ref[t]
        for s in range(slots):
            start = pl.multiple_of(index_ref[t * slots + s] * tile, tile)
            rows = basis_ref[pl.ds(start, tile), :]
            gat_ref[s * tile:(s + 1) * tile, :] = jnp.where(s < live, rows, jnp.zeros_like(rows))
        lhs = jnp.concatenate([tiles_ref[r, s] for s in range(slots)], axis=1)
        out_ref[r] = jnp.dot(lhs, gat_ref[...], preferred_element_type=jnp.float32).astype(out_ref.dtype)


def apply_tiles(tiles, basis, index, counts, rows_per_block=16):
    trows, slots, tile, _ = tiles.shape
    width = basis.shape[-1]
    kernel = functools.partial(_apply_kernel, rows_per_block=rows_per_block, slots=slots, tile=tile)
    spec = pltpu.PrefetchScalarGridSpec(
        num_scalar_prefetch=2,
        grid=(trows // rows_per_block,),
        in_specs=[
            pl.BlockSpec((rows_per_block, slots, tile, tile), lambda i, idx, cnt: (i, 0, 0, 0)),
            pl.BlockSpec(basis.shape, lambda i, idx, cnt: (0, 0)),
        ],
        out_specs=pl.BlockSpec((rows_per_block, tile, width), lambda i, idx, cnt: (i, 0, 0)),
        scratch_shapes=[pltpu.VMEM((slots * tile, width), basis.dtype)],
    )
    return pl.pallas_call(
        kernel,
        grid_spec=spec,
        out_shape=jax.ShapeDtypeStruct((trows, tile, width), jnp.bfloat16),
    )(index.reshape(-1), counts, tiles, basis)


def gather_rows(x, axis):
    n = lax.axis_size(axis)
    got = lax.all_to_all(jnp.broadcast_to(x, (n,) + x.shape), axis, 0, 0, tiled=False)
    return got.reshape((-1,) + x.shape[1:])


def sum_scatter_rows(x, axis):
    n = lax.axis_size(axis)
    got = lax.all_to_all(x.reshape((n, -1) + x.shape[1:]), axis, 0, 0, tiled=False)
    return jnp.sum(got.astype(jnp.float32), axis=0)


def sum_all(x, axes):
    n = 1
    for a in axes:
        n *= lax.axis_size(a)
    piece = jnp.sum(lax.all_to_all(x.reshape(n, -1), axes, 0, 0, tiled=False), axis=0)
    full = lax.all_to_all(jnp.broadcast_to(piece, (n,) + piece.shape), axes, 0, 0, tiled=False)
    return full.reshape(x.shape)


def body(basis, degree_scale, tile_data, tile_index, tile_count):
    tiles = tile_data[:, 0]
    index = tile_index[:, 0]
    counts = tile_count[:, 0]
    rows_dev, width = basis.shape
    tile = tiles.shape[-1]
    nodes = rows_dev * lax.axis_size("row") * lax.axis_size("col")
    scale = degree_scale[:, None]
    probe = (basis.astype(jnp.float32) * scale).astype(jnp.bfloat16)
    number = lax.axis_size("col") * rows_dev // tile
    scale_block = lax.all_gather(degree_scale, "row", axis=0, tiled=True)[:, None]

    def loop_step(i, carry):
        block_probe = carry[0]
        result = apply_tiles(tiles, block_probe, index, counts)
        summed = sum_scatter_rows(result.reshape(number * tile, width), "col")
        image = summed * scale
        gram = sum_all(gram_of(image, nodes), ("row", "col"))
        image_late, gram = lax.optimization_barrier((image, gram))
        image_block = lax.all_gather(image_late, "row", axis=0, tiled=True)
        gram = (gram + gram.T) * 0.5
        lower, inverse = cholesky_and_inverse(gram)

        def probe_of(block, inv):
            normalized = jnp.dot(block, inv.T, precision=lax.Precision.HIGH, preferred_element_type=jnp.float32)
            return (normalized * scale_block).astype(jnp.bfloat16)

        next_probe = lax.cond(
            i < ITERS - 1, probe_of, lambda block, inv: jnp.zeros(block.shape, jnp.bfloat16), image_block, inverse
        )
        return (next_probe, image, inverse, lower)

    square = jnp.zeros((width, width), jnp.float32)
    start = (gather_rows(probe, "row"), jnp.zeros(basis.shape, jnp.float32), square, square)
    _, image, inverse, lower = lax.fori_loop(0, ITERS, loop_step, start)
    embedding = dot_hi(image, inverse.T)
    factor = lower.T
    return (embedding, factor)


def solution(mesh):
    placed = (
        P(("row", "col"), None),
        P(("row", "col")),
        P("row", "col", None, None, None),
        P("row", "col", None),
        P("row", "col"),
    )
    return jax.shard_map(
        body, mesh=mesh, in_specs=placed, out_specs=(P(("row", "col"), None), P()), check_vma=False
    )
```

```python
import functools

import jax
import jax.numpy as jnp
from jax import lax
from jax.experimental import pallas as pl
from jax.experimental.pallas import tpu as pltpu
from jax.sharding import PartitionSpec as P


ITERS = 4


def gram_of(image, nodes):
    return (
        lax.dot_general(
            image,
            image,
            (((0,), (0,)), ((), ())),
            precision=lax.Precision.HIGHEST,
            preferred_element_type=jnp.float32,
        )
        / nodes
    )


def dot_hi(a, b):
    return jnp.dot(a, b, precision=lax.Precision.HIGHEST, preferred_element_type=jnp.float32)


def cholesky_and_inverse(g, leaf=128):
    n = g.shape[0]
    if n <= leaf:
        lower = jnp.linalg.cholesky(g, symmetrize_input=False)
        eye = jnp.eye(n, dtype=jnp.float32)
        return lower, jax.scipy.linalg.solve_triangular(lower, eye, lower=True)
    h = n // 2
    l11, i11 = cholesky_and_inverse(g[:h, :h], leaf)
    l21 = dot_hi(g[h:, :h], i11.T)
    l22, i22 = cholesky_and_inverse(g[h:, h:] - dot_hi(l21, l21.T), leaf)
    i21 = -dot_hi(i22, dot_hi(l21, i11))
    zero = jnp.zeros((h, n - h), jnp.float32)
    lower = jnp.block([[l11, zero], [l21, l22]])
    inverse = jnp.block([[i11, zero], [i21, i22]])
    return lower, inverse


def _apply_kernel(index_ref, count_ref, tiles_ref, basis_ref, out_ref, gat_ref, *, rows_per_block, slots, tile):
    block = pl.program_id(0)
    for r in range(rows_per_block):
        t = block * rows_per_block + r
        live = count_ref[t]
        for s in range(slots):
            start = pl.multiple_of(index_ref[t * slots + s] * tile, tile)
            rows = basis_ref[pl.ds(start, tile), :]
            gat_ref[s * tile:(s + 1) * tile, :] = jnp.where(s < live, rows, jnp.zeros_like(rows))
        lhs = jnp.concatenate([tiles_ref[r, s] for s in range(slots)], axis=1)
        out_ref[r] = jnp.dot(lhs, gat_ref[...], preferred_element_type=jnp.float32).astype(out_ref.dtype)


def apply_tiles(tiles, basis, index, counts, rows_per_block=16):
    trows, slots, tile, _ = tiles.shape
    width = basis.shape[-1]
    kernel = functools.partial(_apply_kernel, rows_per_block=rows_per_block, slots=slots, tile=tile)
    spec = pltpu.PrefetchScalarGridSpec(
        num_scalar_prefetch=2,
        grid=(trows // rows_per_block,),
        in_specs=[
            pl.BlockSpec((rows_per_block, slots, tile, tile), lambda i, idx, cnt: (i, 0, 0, 0)),
            pl.BlockSpec(basis.shape, lambda i, idx, cnt: (0, 0)),
        ],
        out_specs=pl.BlockSpec((rows_per_block, tile, width), lambda i, idx, cnt: (i, 0, 0)),
        scratch_shapes=[pltpu.VMEM((slots * tile, width), basis.dtype)],
    )
    return pl.pallas_call(
        kernel,
        grid_spec=spec,
        out_shape=jax.ShapeDtypeStruct((trows, tile, width), jnp.bfloat16),
    )(index.reshape(-1), counts, tiles, basis)


def gather_rows(x, axis):
    n = lax.axis_size(axis)
    got = lax.all_to_all(jnp.broadcast_to(x, (n,) + x.shape), axis, 0, 0, tiled=False)
    return got.reshape((-1,) + x.shape[1:])


def sum_scatter_rows(x, axis):
    n = lax.axis_size(axis)
    got = lax.all_to_all(x.reshape((n, -1) + x.shape[1:]), axis, 0, 0, tiled=False)
    return jnp.sum(got.astype(jnp.float32), axis=0)


def sum_all(x, axes):
    n = 1
    for a in axes:
        n *= lax.axis_size(a)
    piece = jnp.sum(lax.all_to_all(x.reshape(n, -1), axes, 0, 0, tiled=False), axis=0)
    full = lax.all_to_all(jnp.broadcast_to(piece, (n,) + piece.shape), axes, 0, 0, tiled=False)
    return full.reshape(x.shape)


def body(basis, degree_scale, tile_data, tile_index, tile_count):
    tiles = tile_data[:, 0]
    index = tile_index[:, 0]
    counts = tile_count[:, 0]
    rows_dev, width = basis.shape
    tile = tiles.shape[-1]
    nodes = rows_dev * lax.axis_size("row") * lax.axis_size("col")
    scale = degree_scale[:, None]
    probe = (basis.astype(jnp.float32) * scale).astype(jnp.bfloat16)
    number = lax.axis_size("col") * rows_dev // tile
    scale_block = lax.all_gather(degree_scale, "row", axis=0, tiled=True)[:, None]

    def loop_step(i, carry):
        block_probe = carry[0]
        result = apply_tiles(tiles, block_probe, index, counts)
        summed = sum_scatter_rows(result.reshape(number * tile, width), "col")
        image = summed * scale
        gram = sum_all(gram_of(image, nodes), ("row", "col"))
        image_late, gram = lax.optimization_barrier((image, gram))
        image_block = lax.all_gather(image_late, "row", axis=0, tiled=True)
        lower, inverse = cholesky_and_inverse(gram)
        normalized = jnp.dot(image_block, inverse.T, precision=lax.Precision.HIGH, preferred_element_type=jnp.float32)
        next_probe = (normalized * scale_block).astype(jnp.bfloat16)
        return (next_probe, image, inverse, lower)

    square = jnp.zeros((width, width), jnp.float32)
    start = (gather_rows(probe, "row"), jnp.zeros(basis.shape, jnp.float32), square, square)
    _, image, inverse, lower = lax.fori_loop(0, ITERS, loop_step, start)
    embedding = dot_hi(image, inverse.T)
    factor = lower.T
    return (embedding, factor)


def solution(mesh):
    placed = (
        P(("row", "col"), None),
        P(("row", "col")),
        P("row", "col", None, None, None),
        P("row", "col", None),
        P("row", "col"),
    )
    return jax.shard_map(
        body, mesh=mesh, in_specs=placed, out_specs=(P(("row", "col"), None), P()), check_vma=False
    )
```

```python
import functools

import jax
import jax.numpy as jnp
from jax import lax
from jax.experimental import pallas as pl
from jax.experimental.pallas import tpu as pltpu
from jax.sharding import PartitionSpec as P


ITERS = 4


def gram_of(image, nodes):
    return (
        lax.dot_general(
            image,
            image,
            (((0,), (0,)), ((), ())),
            precision=lax.Precision.HIGHEST,
            preferred_element_type=jnp.float32,
        )
        / nodes
    )


def dot_hi(a, b):
    return jnp.dot(a, b, precision=lax.Precision.HIGHEST, preferred_element_type=jnp.float32)


def cholesky_and_inverse(g, leaf=128):
    n = g.shape[0]
    if n <= leaf:
        lower = jnp.linalg.cholesky(g, symmetrize_input=False)
        eye = jnp.eye(n, dtype=jnp.float32)
        return lower, jax.scipy.linalg.solve_triangular(lower, eye, lower=True)
    h = n // 2
    l11, i11 = cholesky_and_inverse(g[:h, :h], leaf)
    l21 = dot_hi(g[h:, :h], i11.T)
    l22, i22 = cholesky_and_inverse(g[h:, h:] - dot_hi(l21, l21.T), leaf)
    i21 = -dot_hi(i22, dot_hi(l21, i11))
    zero = jnp.zeros((h, n - h), jnp.float32)
    lower = jnp.block([[l11, zero], [l21, l22]])
    inverse = jnp.block([[i11, zero], [i21, i22]])
    return lower, inverse


def _apply_kernel(index_ref, count_ref, tiles_ref, basis_ref, out_ref, gat_ref, *, rows_per_block, slots, tile):
    block = pl.program_id(0)
    for r in range(rows_per_block):
        t = block * rows_per_block + r
        live = count_ref[t]
        for s in range(slots):
            start = pl.multiple_of(index_ref[t * slots + s] * tile, tile)
            rows = basis_ref[pl.ds(start, tile), :]
            gat_ref[s * tile:(s + 1) * tile, :] = jnp.where(s < live, rows, jnp.zeros_like(rows))
        lhs = jnp.concatenate([tiles_ref[r, s] for s in range(slots)], axis=1)
        out_ref[r] = jnp.dot(lhs, gat_ref[...], preferred_element_type=jnp.float32).astype(out_ref.dtype)


def apply_tiles(tiles, basis, index, counts, rows_per_block=16):
    trows, slots, tile, _ = tiles.shape
    width = basis.shape[-1]
    kernel = functools.partial(_apply_kernel, rows_per_block=rows_per_block, slots=slots, tile=tile)
    spec = pltpu.PrefetchScalarGridSpec(
        num_scalar_prefetch=2,
        grid=(trows // rows_per_block,),
        in_specs=[
            pl.BlockSpec((rows_per_block, slots, tile, tile), lambda i, idx, cnt: (i, 0, 0, 0)),
            pl.BlockSpec(basis.shape, lambda i, idx, cnt: (0, 0)),
        ],
        out_specs=pl.BlockSpec((rows_per_block, tile, width), lambda i, idx, cnt: (i, 0, 0)),
        scratch_shapes=[pltpu.VMEM((slots * tile, width), basis.dtype)],
    )
    return pl.pallas_call(
        kernel,
        grid_spec=spec,
        out_shape=jax.ShapeDtypeStruct((trows, tile, width), jnp.bfloat16),
    )(index.reshape(-1), counts, tiles, basis)


def sum_scatter_rows(x, axis):
    n = lax.axis_size(axis)
    got = lax.all_to_all(x.reshape((n, -1) + x.shape[1:]), axis, 0, 0, tiled=False)
    return jnp.sum(got.astype(jnp.float32), axis=0)


def sum_all(x, axes):
    n = 1
    for a in axes:
        n *= lax.axis_size(a)
    piece = jnp.sum(lax.all_to_all(x.reshape(n, -1), axes, 0, 0, tiled=False), axis=0)
    full = lax.all_to_all(jnp.broadcast_to(piece, (n,) + piece.shape), axes, 0, 0, tiled=False)
    return full.reshape(x.shape)


def body(basis, degree_scale, tile_data, tile_index, tile_count):
    tiles = tile_data[:, 0]
    index = tile_index[:, 0]
    counts = tile_count[:, 0]
    rows_dev, width = basis.shape
    tile = tiles.shape[-1]
    nodes = rows_dev * lax.axis_size("row") * lax.axis_size("col")
    scale = degree_scale[:, None]
    probe = (basis.astype(jnp.float32) * scale).astype(jnp.bfloat16)
    number = lax.axis_size("col") * rows_dev // tile
    scale_block = lax.all_gather(degree_scale, "row", axis=0, tiled=True)[:, None]

    def loop_step(i, carry):
        block_probe = carry[0]
        result = apply_tiles(tiles, block_probe, index, counts)
        summed = sum_scatter_rows(result.reshape(number * tile, width), "col")
        image = summed * scale
        gram = sum_all(gram_of(image, nodes), ("row", "col"))
        image_late, gram = lax.optimization_barrier((image, gram))
        image_block = lax.all_gather(image_late, "row", axis=0, tiled=True)
        lower, inverse = cholesky_and_inverse(gram)
        normalized = jnp.dot(image_block, inverse.T, precision=lax.Precision.HIGH, preferred_element_type=jnp.float32)
        next_probe = (normalized * scale_block).astype(jnp.bfloat16)
        return (next_probe, image, inverse, lower)

    square = jnp.zeros((width, width), jnp.float32)
    start = (lax.all_gather(probe, "row", axis=0, tiled=True), jnp.zeros(basis.shape, jnp.float32), square, square)
    _, image, inverse, lower = lax.fori_loop(0, ITERS, loop_step, start)
    embedding = dot_hi(image, inverse.T)
    factor = lower.T
    return (embedding, factor)


def solution(mesh):
    placed = (
        P(("row", "col"), None),
        P(("row", "col")),
        P("row", "col", None, None, None),
        P("row", "col", None),
        P("row", "col"),
    )
    return jax.shard_map(
        body, mesh=mesh, in_specs=placed, out_specs=(P(("row", "col"), None), P()), check_vma=False
    )
```
